512 devices in a mesh: site: 32 (over z_hi, y, core), shard: 16 (over x, z_lo).
Axes of the slice: x: 4, y: 4, z: 16 (z_hi: 4, z_lo: 4; z = z_hi * 4 + z_lo), core: 2. Of those that a mesh axis runs over, the one named last changes fastest.
Arguments:
- activations: bfloat16 [65536, 2560], P(('site', 'shard')), may hold values from -6 to 6
- out_grads: bfloat16 [65536, 5120], P(('site', 'shard')), may hold values from -6 to 6
- theta: bfloat16 [32, 2560, 5120], P('site', None, 'shard'), may hold values from -6 to 6
- token_ids: int32 [65536], P(('site', 'shard')), may hold values from 0 to 31999
- assignment: int32 [32, 2048], P('site'), may hold values from 0 to 2047, each once within a row
Outputs:
- merged: bfloat16 [2560, 5120], P('site', 'shard')
- response: bfloat16 [16384, 5120], P('site', 'shard')
The draws below stay inside these ranges and needn't reach their ends.
Inputs may be any that keep to these rules, and one draw needn't show every extreme that they name: Each row of assignment holds every site position 0 to 2047 once.
All inputs are finite; a program needn't handle non-finite values.
Results may differ from the reference program's by a relative error of at most 0.02.
Values may be sent and summed in bfloat16 or wider, within the bound.
No kernel may reach another device: no remote copies, remote signals or barrier semaphores. Data moves between devices by JAX's collectives and lax.ppermute only.
A program may use at most 64 MiB of HBM per device.

```python
import math
import jax
import jax.numpy as jnp
import numpy as np
from jax import lax

D = 5120
HEADS = 20
HEAD_DIM = 128
VOCAB = 32000
MICRO = 4
HD = 2560
E_SITE = 2048
MB = 512
EVENTS = 65536
N_SITE = 32


def touch_ends(array, own_key, smallest, largest):
    longest = array.shape.index(max(array.shape))
    spots = []
    for shift in (0, 1):
        where = [jax.random.randint(jax.random.fold_in(own_key, axis), (), 0, length) for axis, length in enumerate(array.shape)]
        where[longest] = (where[longest] + shift) % array.shape[longest]
        spots.append(tuple(where))
    return array.at[spots[0]].set(smallest).at[spots[1]].set(largest)


def raised(result, stream_key, source, target, parts, factor):
    def block_of(dim):
        return (jnp.arange(result.shape[dim]) // (result.shape[dim] // parts)).reshape((-1,) + (1,) * (result.ndim - 1 - dim))

    one_side = jax.random.permutation(stream_key, parts)[block_of(target)]
    far = (block_of(target) + parts // 2) % parts
    return jnp.where((block_of(source) == one_side) | (block_of(source) == far), factor * result, result)


def level_of(key, dims, pieces, least, high):
    def one(axis_at, parts):
        heights = jax.random.uniform(jax.random.fold_in(jax.random.fold_in(key, 6), axis_at), (parts,), jnp.float32, least / len(pieces), high / len(pieces))
        return jnp.repeat(jnp.exp(heights), dims[axis_at] // parts).reshape((-1,) + (1,) * (len(dims) - axis_at - 1))

    gain = one(*pieces[0])
    for cut in pieces[1:]:
        gain = gain * one(*cut)
    return gain


def cumulative_ranks(count, slope):
    portions = [(1 << 20) // math.isqrt(rank ** slope) + 1 for rank in range(1, count + 1)]
    scale = 1 + sum(portions) // (1 << 30)
    return np.cumsum(np.array([max(1, weight // scale) for weight in portions]))


def ranked_ids(key, dims, amount, slope):
    listing = cumulative_ranks(amount, slope)
    pick = jax.random.randint(jax.random.fold_in(key, 1), dims, 0, int(listing[amount - 1]))
    standing = jnp.searchsorted(jnp.asarray(listing, jnp.int32), pick, side="right")
    return jax.random.permutation(jax.random.fold_in(key, 2), amount)[standing].astype(jnp.int32)


def normal_values(key, extent, deviation, most, split=(), held_as=jnp.bfloat16):
    gain = level_of(key, extent, split, -0.22, 0.18) if split else 1.0
    entries = jax.random.normal(key, extent, jnp.float32) * deviation * gain
    return jnp.minimum(jnp.maximum(entries, -most), most).astype(held_as)


def heavy_noise(stream_key, dims, deviation, limit, pieces, heavy, held_as=jnp.bfloat16):
    drawn = deviation * jax.random.normal(stream_key, dims, jnp.float32)
    if pieces:
        drawn = drawn * level_of(stream_key, dims, pieces, -0.22, 0.18)
    return jnp.clip(raised(drawn, jax.random.fold_in(stream_key, 3), *heavy), -limit, limit).astype(held_as)


def setup_inputs(seed: int = 0) -> dict:
    seeds = jax.random.split(jax.random.key(seed), 6)
    activations = normal_values(seeds[0], (EVENTS, HD), 1.0, 6.0, ((0, 512),))
    out_grads = normal_values(seeds[1], (EVENTS, D), 1.0, 6.0, ((0, 512),))
    theta = heavy_noise(seeds[2], (N_SITE, HD, D), 1.0, 6.0, ((0, 32), (2, 16)), (0, 1, 32, 2.75))
    token_ids = touch_ends(ranked_ids(seeds[3], (EVENTS,), VOCAB, 2), jax.random.fold_in(seeds[3], 3), 0, VOCAB - 1).astype(jnp.int32)
    assignment = jax.vmap(lambda own: jax.random.permutation(own, E_SITE))(jax.random.split(seeds[4], N_SITE)).reshape((N_SITE, E_SITE)).astype(jnp.int32)
    return dict(activations=activations, out_grads=out_grads, theta=theta, token_ids=token_ids, assignment=assignment)


epsilon = 1e-6


def round_trip(values):
    return lax.optimization_barrier(values.astype(jnp.bfloat16)).astype(jnp.float32)


def reference(activations, out_grads, theta, token_ids, assignment):
    head_cols = HEADS * HEAD_DIM
    site_acts = activations.reshape(N_SITE, E_SITE, head_cols)
    site_grads = out_grads.reshape(N_SITE, E_SITE, D)
    site_ids = token_ids.reshape(N_SITE, E_SITE)

    def one_site(carry, inputs):
        numerator, denominator = carry
        acts_one, grads_one, ids_one, ordering, theta_one = inputs
        counts = jnp.sum((ids_one[:, None] == ids_one[None, :]).astype(jnp.int32), axis=1)
        weights = 1.0 / counts.astype(jnp.float32)
        fisher = jnp.zeros((head_cols, D), jnp.float32)
        for micro in range(MICRO):
            picked = ordering[micro * MB:(micro + 1) * MB]
            acts_micro = acts_one[picked]
            scaled = (grads_one[picked].astype(jnp.float32) * weights[picked][:, None]).astype(jnp.bfloat16)
            gradient = jnp.dot(acts_micro.T, scaled, preferred_element_type=jnp.float32)
            fisher = fisher + gradient * gradient
        fisher = fisher / MICRO
        product = fisher * theta_one.astype(jnp.float32)
        return (numerator + round_trip(product), denominator + round_trip(fisher)), None

    start = (jnp.zeros((head_cols, D), jnp.float32), jnp.zeros((head_cols, D), jnp.float32))
    (numerator, denominator), unused = lax.scan(one_site, start, (site_acts, site_grads, site_ids, assignment, theta))
    merged = (numerator / (denominator + epsilon)).astype(jnp.bfloat16)
    scaling = float(head_cols) ** -0.5

    def probe_site(carry, inputs):
        acts_one, ordering = inputs
        probe = acts_one[ordering[:MB]]
        answer = (jnp.dot(probe, merged, preferred_element_type=jnp.float32) * scaling).astype(jnp.bfloat16)
        return carry, answer

    unused_carry, response = lax.scan(probe_site, jnp.zeros((), jnp.float32), (site_acts, assignment))
    return merged, response.reshape(N_SITE * MB, D)
```

```python
import math

import jax
import jax.numpy as jnp
import numpy as np
from jax import lax
from jax.sharding import Mesh
from jax.sharding import PartitionSpec as P

HEADS = 20
HEAD_DIM = 128
MICRO = 4


epsilon = 1e-06

SITE_SUB = (("zh", 4), ("y", 4), ("c", 2))
SHARD_SUB = (("x", 4), ("zl", 4))


def count_same(site_ids):
    site_events = site_ids.shape[0]
    block_rows = math.gcd(site_events, 512)
    blocks = site_ids.reshape(site_events // block_rows, block_rows)

    def one_block(block_ids):
        return jnp.sum((block_ids[:, None] == site_ids[None, :]).astype(jnp.int32), axis=1)

    return lax.map(one_block, blocks).reshape(site_events)


def make_body(site_axes, shard_axes):
    site_names = tuple(n for n, _ in site_axes)
    site_sizes = tuple(s for _, s in site_axes)
    shard_names = tuple(n for n, _ in shard_axes)

    def gather_events(x):
        for name in reversed(shard_names):
            x = lax.all_gather(x, name, axis=0, tiled=True)
        return x

    def scatter_sites(x):
        rows = x.shape[0]
        n = len(site_sizes)
        x = x.reshape(site_sizes + (rows // math.prod(site_sizes),) + x.shape[1:])
        x = jnp.transpose(x, tuple(reversed(range(n))) + tuple(range(n, x.ndim)))
        x = x.reshape((rows,) + x.shape[n + 1 :])
        for name in reversed(site_names):
            x = lax.psum_scatter(x, name, scatter_dimension=0, tiled=True)
        return x

    def gather_sites(x):
        for name in site_names:
            x = lax.all_gather(x, name, axis=0, tiled=True)
        n = len(site_sizes)
        rows = x.shape[0]
        x = x.reshape(tuple(reversed(site_sizes)) + (rows // math.prod(site_sizes),) + x.shape[1:])
        x = jnp.transpose(x, tuple(reversed(range(n))) + tuple(range(n, x.ndim)))
        return x.reshape((rows,) + x.shape[n + 1 :])

    def on_device(activations, out_grads, theta, token_ids, assignment):
        head_cols = HEADS * HEAD_DIM
        site_ids = lax.all_gather(token_ids, shard_names, axis=0, tiled=True)
        site_acts = gather_events(activations)
        grad_cols = lax.all_to_all(out_grads, shard_names, split_axis=1, concat_axis=0, tiled=True)
        site_events = site_acts.shape[0]
        micro_rows = site_events // MICRO
        ordering = assignment[0]
        counts = count_same(site_ids)
        weights = 1.0 / counts.astype(jnp.float32)
        scaled = (grad_cols.astype(jnp.float32) * weights[:, None]).astype(jnp.bfloat16)
        position_batch = (jnp.arange(site_events, dtype=jnp.int32) // micro_rows)[None, :]
        hit = ordering[None, :] == jnp.arange(site_events, dtype=jnp.int32)[:, None]
        batch_of = jnp.sum(jnp.where(hit, position_batch, 0), axis=1)
        masked = jnp.concatenate(
            [jnp.where((batch_of == m)[:, None], scaled, jnp.zeros_like(scaled)) for m in range(MICRO)],
            axis=1,
        )
        gradients = lax.dot_general(
            site_acts, masked, (((0,), (0,)), ((), ())), preferred_element_type=jnp.float32
        )
        cols = scaled.shape[1]
        fisher = gradients[:, :cols] * gradients[:, :cols]
        for micro in range(1, MICRO):
            g = gradients[:, micro * cols : (micro + 1) * cols]
            fisher = fisher + g * g
        fisher = fisher / MICRO
        product = fisher * theta[0].astype(jnp.float32)
        both = jnp.concatenate([product.astype(jnp.bfloat16), fisher.astype(jnp.bfloat16)], axis=1)
        summed = scatter_sites(both).astype(jnp.float32)
        numerator, denominator = summed[:, :cols], summed[:, cols:]
        owned = (numerator / (denominator + epsilon)).astype(jnp.bfloat16)
        whole_merged = gather_sites(owned)
        scaling = float(head_cols) ** (-0.5)
        answers = (
            jnp.dot(site_acts, whole_merged, preferred_element_type=jnp.float32) * scaling
        ).astype(jnp.bfloat16)
        response = jnp.take(answers, ordering[:micro_rows], axis=0)
        return (owned, response)

    return on_device


def solution(mesh):
    sizes = dict(mesh.shape)
    site_ok = math.prod(s for _, s in SITE_SUB) == sizes["site"]
    shard_ok = math.prod(s for _, s in SHARD_SUB) == sizes["shard"]
    if site_ok and shard_ok:
        site_axes, shard_axes = SITE_SUB, SHARD_SUB
        shape = tuple(s for _, s in SITE_SUB + SHARD_SUB)
        names = tuple(n for n, _ in SITE_SUB + SHARD_SUB)
        use_mesh = Mesh(np.asarray(mesh.devices).reshape(shape), names)
    else:
        site_axes, shard_axes = (("site", sizes["site"]),), (("shard", sizes["shard"]),)
        use_mesh = mesh
    site = tuple(n for n, _ in site_axes)
    shard = tuple(n for n, _ in shard_axes)
    placed = (
        P(site + shard, None),
        P(site + shard, None),
        P(site, None, shard),
        P(site + shard),
        P(site, None),
    )
    return jax.shard_map(
        make_body(site_axes, shard_axes),
        mesh=use_mesh,
        in_specs=placed,
        out_specs=(P(site, shard), P(site, shard)),
        check_vma=False,
    )
```

```python
import math

import jax
import jax.numpy as jnp
import numpy as np
from jax import lax
from jax.sharding import Mesh
from jax.sharding import PartitionSpec as P

HEADS = 20
HEAD_DIM = 128
MICRO = 4


epsilon = 1e-06

SITE_SUB = (("zh", 4), ("y", 4), ("c", 2))
SHARD_SUB = (("x", 4), ("zl", 4))
SCATTER_STAGES = (("y", "c"), ("zh",))


def count_same(site_ids):
    site_events = site_ids.shape[0]
    block_rows = math.gcd(site_events, 512)
    blocks = site_ids.reshape(site_events // block_rows, block_rows)

    def one_block(block_ids):
        return jnp.sum((block_ids[:, None] == site_ids[None, :]).astype(jnp.int32), axis=1)

    return lax.map(one_block, blocks).reshape(site_events)


def make_body(site_axes, shard_axes, scatter_stages):
    site_names = tuple(n for n, _ in site_axes)
    site_sizes = tuple(s for _, s in site_axes)
    shard_names = tuple(n for n, _ in shard_axes)
    position_names = tuple(n for stage in scatter_stages for n in stage)
    position_axes = tuple(site_names.index(n) for n in position_names)
    n_sub = len(site_sizes)

    def to_position_order(x, axis):
        shape = x.shape
        block = shape[axis] // math.prod(site_sizes)
        x = x.reshape(shape[:axis] + site_sizes + (block,) + shape[axis + 1 :])
        order = (
            tuple(range(axis))
            + tuple(axis + a for a in position_axes)
            + tuple(range(axis + n_sub, x.ndim))
        )
        return jnp.transpose(x, order).reshape(shape)

    def gather_events(x):
        for name in reversed(shard_names):
            x = lax.all_gather(x, name, axis=0, tiled=True)
        return x

    def scatter_sites(x):
        for stage in scatter_stages:
            x = lax.psum_scatter(x, stage, scatter_dimension=0, tiled=True)
        return x

    def gather_sites(x):
        for stage in reversed(scatter_stages):
            x = lax.all_gather(x, stage, axis=0, tiled=True)
        return x

    def on_device(activations, out_grads, theta, token_ids, assignment):
        head_cols = HEADS * HEAD_DIM
        site_ids = lax.all_gather(token_ids, shard_names, axis=0, tiled=True)
        site_acts = gather_events(to_position_order(activations, 1))
        grad_cols = lax.all_to_all(out_grads, shard_names, split_axis=1, concat_axis=0, tiled=True)
        theta_rows = to_position_order(theta[0], 0)
        site_events = site_acts.shape[0]
        micro_rows = site_events // MICRO
        ordering = assignment[0]
        counts = count_same(site_ids)
        weights = 1.0 / counts.astype(jnp.float32)
        scaled = (grad_cols.astype(jnp.float32) * weights[:, None]).astype(jnp.bfloat16)
        position_batch = (jnp.arange(site_events, dtype=jnp.int32) // micro_rows)[None, :]
        hit = ordering[None, :] == jnp.arange(site_events, dtype=jnp.int32)[:, None]
        batch_of = jnp.sum(jnp.where(hit, position_batch, 0), axis=1)
        masked = jnp.concatenate(
            [jnp.where((batch_of == m)[:, None], scaled, jnp.zeros_like(scaled)) for m in range(MICRO)],
            axis=1,
        )
        gradients = lax.dot_general(
            site_acts, masked, (((0,), (0,)), ((), ())), preferred_element_type=jnp.float32
        )
        cols = scaled.shape[1]
        fisher = gradients[:, :cols] * gradients[:, :cols]
        for micro in range(1, MICRO):
            g = gradients[:, micro * cols : (micro + 1) * cols]
            fisher = fisher + g * g
        fisher = fisher / MICRO
        product = fisher * theta_rows.astype(jnp.float32)
        both = jnp.concatenate([product.astype(jnp.bfloat16), fisher.astype(jnp.bfloat16)], axis=1)
        summed = scatter_sites(both).astype(jnp.float32)
        numerator, denominator = summed[:, :cols], summed[:, cols:]
        owned = (numerator / (denominator + epsilon)).astype(jnp.bfloat16)
        whole_merged = gather_sites(owned)
        scaling = float(head_cols) ** (-0.5)
        probe = jnp.take(site_acts, ordering[:micro_rows], axis=0)
        response = (
            jnp.dot(probe, whole_merged, preferred_element_type=jnp.float32) * scaling
        ).astype(jnp.bfloat16)
        return (owned, response)

    return on_device


def solution(mesh):
    sizes = dict(mesh.shape)
    site_ok = math.prod(s for _, s in SITE_SUB) == sizes["site"]
    shard_ok = math.prod(s for _, s in SHARD_SUB) == sizes["shard"]
    if site_ok and shard_ok:
        site_axes, shard_axes = SITE_SUB, SHARD_SUB
        scatter_stages = SCATTER_STAGES
        shape = tuple(s for _, s in SITE_SUB + SHARD_SUB)
        names = tuple(n for n, _ in SITE_SUB + SHARD_SUB)
        use_mesh = Mesh(np.asarray(mesh.devices).reshape(shape), names)
    else:
        site_axes, shard_axes = (("site", sizes["site"]),), (("shard", sizes["shard"]),)
        scatter_stages = (("site",),)
        use_mesh = mesh
    site = tuple(n for n, _ in site_axes)
    shard = tuple(n for n, _ in shard_axes)
    placed = (
        P(site + shard, None),
        P(site + shard, None),
        P(site, None, shard),
        P(site + shard),
        P(site, None),
    )
    return jax.shard_map(
        make_body(site_axes, shard_axes, scatter_stages),
        mesh=use_mesh,
        in_specs=placed,
        out_specs=(P(site, shard), P(site, shard)),
        check_vma=False,
    )
```

```python
import math

import jax
import jax.numpy as jnp
import numpy as np
from jax import lax
from jax.sharding import Mesh
from jax.sharding import PartitionSpec as P

HEADS = 20
HEAD_DIM = 128
MICRO = 4


epsilon = 1e-06

SITE_SUB = (("zh", 4), ("y", 4), ("c", 2))
SHARD_SUB = (("x", 4), ("zl", 4))
SCATTER_STAGES = (("y", "c"), ("zh",))
SHARD_KINDS = ("ring4", "line")


def count_same(site_ids):
    site_events = site_ids.shape[0]
    block_rows = math.gcd(site_events, 512)
    blocks = site_ids.reshape(site_events // block_rows, block_rows)

    def one_block(block_ids):
        return jnp.sum((block_ids[:, None] == site_ids[None, :]).astype(jnp.int32), axis=1)

    return lax.map(one_block, blocks).reshape(site_events)


def place_blocks(parts, n, rows):
    shape = ((n + 1) * rows,) + parts[0][0].shape[1:]
    out = jnp.zeros(shape, parts[0][0].dtype)
    for value, block in parts:
        start = (block * rows,) + (0,) * (value.ndim - 1)
        out = lax.dynamic_update_slice(out, value, start)
    return out[: n * rows]


def line_gather(xs, name, n):
    i = lax.axis_index(name)
    rows = xs[0].shape[0]
    right, left = [xs], [xs]
    for step in range(1, n):
        to_right = [(k, k + 1) for k in range(step - 1, n - 1)]
        to_left = [(k, k - 1) for k in range(1, n - step + 1)]
        right.append(tuple(lax.ppermute(x, name, to_right) for x in right[-1]))
        left.append(tuple(lax.ppermute(x, name, to_left) for x in left[-1]))
    outs = []
    for a in range(len(xs)):
        parts = [(xs[a], i)]
        for step in range(1, n):
            parts.append((right[step][a], jnp.where(i - step >= 0, i - step, n)))
            parts.append((left[step][a], jnp.where(i + step <= n - 1, i + step, n)))
        outs.append(place_blocks(parts, n, rows))
    return tuple(outs)


def ring4_gather(xs, name):
    n = 4
    i = lax.axis_index(name)
    rows = xs[0].shape[0]
    half = rows // 2
    fw = [(k, (k + 1) % n) for k in range(n)]
    bw = [(k, (k - 1) % n) for k in range(n)]
    from_left = tuple(lax.ppermute(x, name, fw) for x in xs)
    from_right = tuple(lax.ppermute(x, name, bw) for x in xs)
    far_first = tuple(lax.ppermute(x[:half], name, fw) for x in from_left)
    far_second = tuple(lax.ppermute(x[half:], name, bw) for x in from_right)
    outs = []
    for a in range(len(xs)):
        shape = (n * rows,) + xs[a].shape[1:]
        out = jnp.zeros(shape, xs[a].dtype)
        zeros = (0,) * (xs[a].ndim - 1)
        out = lax.dynamic_update_slice(out, xs[a], (i * rows,) + zeros)
        out = lax.dynamic_update_slice(out, from_left[a], (((i + n - 1) % n) * rows,) + zeros)
        out = lax.dynamic_update_slice(out, from_right[a], (((i + 1) % n) * rows,) + zeros)
        out = lax.dynamic_update_slice(out, far_first[a], (((i + 2) % n) * rows,) + zeros)
        out = lax.dynamic_update_slice(out, far_second[a], (((i + 2) % n) * rows + half,) + zeros)
        outs.append(out)
    return tuple(outs)


def make_body(site_axes, shard_axes, shard_kinds, scatter_stages):
    site_names = tuple(n for n, _ in site_axes)
    site_sizes = tuple(s for _, s in site_axes)
    shard_names = tuple(n for n, _ in shard_axes)
    position_names = tuple(n for stage in scatter_stages for n in stage)
    position_axes = tuple(site_names.index(n) for n in position_names)
    n_sub = len(site_sizes)

    def to_position_order(x, axis):
        shape = x.shape
        block = shape[axis] // math.prod(site_sizes)
        x = x.reshape(shape[:axis] + site_sizes + (block,) + shape[axis + 1 :])
        order = (
            tuple(range(axis))
            + tuple(axis + a for a in position_axes)
            + tuple(range(axis + n_sub, x.ndim))
        )
        return jnp.transpose(x, order).reshape(shape)

    def gather_events(xs):
        for (name, size), kind in zip(reversed(shard_axes), reversed(shard_kinds)):
            if kind == "line":
                xs = line_gather(xs, name, size)
            elif kind == "ring4":
                xs = ring4_gather(xs, name)
            else:
                xs = tuple(lax.all_gather(x, name, axis=0, tiled=True) for x in xs)
        return xs

    def scatter_sites(x):
        for stage in scatter_stages:
            x = lax.psum_scatter(x, stage, scatter_dimension=0, tiled=True)
        return x

    def gather_sites(x):
        for stage in reversed(scatter_stages):
            x = lax.all_gather(x, stage, axis=0, tiled=True)
        return x

    def on_device(activations, out_grads, theta, token_ids, assignment):
        head_cols = HEADS * HEAD_DIM
        site_acts, site_ids = gather_events((to_position_order(activations, 1), token_ids))
        grad_cols = lax.all_to_all(out_grads, shard_names, split_axis=1, concat_axis=0, tiled=True)
        theta_rows = to_position_order(theta[0], 0)
        site_events = site_acts.shape[0]
        micro_rows = site_events // MICRO
        ordering = assignment[0]
        counts = count_same(site_ids)
        weights = 1.0 / counts.astype(jnp.float32)
        scaled = (grad_cols.astype(jnp.float32) * weights[:, None]).astype(jnp.bfloat16)
        position_batch = (jnp.arange(site_events, dtype=jnp.int32) // micro_rows)[None, :]
        hit = ordering[None, :] == jnp.arange(site_events, dtype=jnp.int32)[:, None]
        batch_of = jnp.sum(jnp.where(hit, position_batch, 0), axis=1)
        masked = jnp.concatenate(
            [jnp.where((batch_of == m)[:, None], scaled, jnp.zeros_like(scaled)) for m in range(MICRO)],
            axis=1,
        )
        gradients = lax.dot_general(
            site_acts, masked, (((0,), (0,)), ((), ())), preferred_element_type=jnp.float32
        )
        cols = scaled.shape[1]
        fisher = gradients[:, :cols] * gradients[:, :cols]
        for micro in range(1, MICRO):
            g = gradients[:, micro * cols : (micro + 1) * cols]
            fisher = fisher + g * g
        fisher = fisher / MICRO
        product = fisher * theta_rows.astype(jnp.float32)
        both = jnp.concatenate([product.astype(jnp.bfloat16), fisher.astype(jnp.bfloat16)], axis=1)
        summed = scatter_sites(both).astype(jnp.float32)
        numerator, denominator = summed[:, :cols], summed[:, cols:]
        owned = (numerator / (denominator + epsilon)).astype(jnp.bfloat16)
        whole_merged = gather_sites(owned)
        scaling = float(head_cols) ** (-0.5)
        probe = jnp.take(site_acts, ordering[:micro_rows], axis=0)
        response = (
            jnp.dot(probe, whole_merged, preferred_element_type=jnp.float32) * scaling
        ).astype(jnp.bfloat16)
        return (owned, response)

    return on_device


def solution(mesh):
    sizes = dict(mesh.shape)
    site_ok = math.prod(s for _, s in SITE_SUB) == sizes["site"]
    shard_ok = math.prod(s for _, s in SHARD_SUB) == sizes["shard"]
    if site_ok and shard_ok:
        site_axes, shard_axes = SITE_SUB, SHARD_SUB
        scatter_stages = SCATTER_STAGES
        shard_kinds = SHARD_KINDS
        shape = tuple(s for _, s in SITE_SUB + SHARD_SUB)
        names = tuple(n for n, _ in SITE_SUB + SHARD_SUB)
        use_mesh = Mesh(np.asarray(mesh.devices).reshape(shape), names)
    else:
        site_axes, shard_axes = (("site", sizes["site"]),), (("shard", sizes["shard"]),)
        scatter_stages = (("site",),)
        shard_kinds = ("collective",)
        use_mesh = mesh
    site = tuple(n for n, _ in site_axes)
    shard = tuple(n for n, _ in shard_axes)
    placed = (
        P(site + shard, None),
        P(site + shard, None),
        P(site, None, shard),
        P(site + shard),
        P(site, None),
    )
    return jax.shard_map(
        make_body(site_axes, shard_axes, shard_kinds, scatter_stages),
        mesh=use_mesh,
        in_specs=placed,
        out_specs=(P(site, shard), P(site, shard)),
        check_vma=False,
    )
```

```python
import math

import jax
import jax.numpy as jnp
import numpy as np
from jax import lax
from jax.sharding import Mesh
from jax.sharding import PartitionSpec as P

HEADS = 20
HEAD_DIM = 128
MICRO = 4


epsilon = 1e-06

SITE_SUB = (("zh", 4), ("y", 4), ("c", 2))
SHARD_SUB = (("x", 4), ("zl", 4))
SCATTER_STAGES = (("y", "c"), ("zh",))
FEATURE_PIECES = 2


def count_same(site_ids):
    site_events = site_ids.shape[0]
    block_rows = math.gcd(site_events, 512)
    blocks = site_ids.reshape(site_events // block_rows, block_rows)

    def one_block(block_ids):
        return jnp.sum((block_ids[:, None] == site_ids[None, :]).astype(jnp.int32), axis=1)

    return lax.map(one_block, blocks).reshape(site_events)


def make_body(site_axes, shard_axes, scatter_stages):
    site_names = tuple(n for n, _ in site_axes)
    site_sizes = tuple(s for _, s in site_axes)
    shard_names = tuple(n for n, _ in shard_axes)
    position_names = tuple(n for stage in scatter_stages for n in stage)
    position_axes = tuple(site_names.index(n) for n in position_names)
    n_sub = len(site_sizes)

    def to_position_order(x, axis):
        shape = x.shape
        block = shape[axis] // math.prod(site_sizes)
        x = x.reshape(shape[:axis] + site_sizes + (block,) + shape[axis + 1 :])
        order = (
            tuple(range(axis))
            + tuple(axis + a for a in position_axes)
            + tuple(range(axis + n_sub, x.ndim))
        )
        return jnp.transpose(x, order).reshape(shape)

    def gather_events(x, pieces):
        names = tuple(reversed(shard_names))
        for name in names[:-1]:
            x = lax.all_gather(x, name, axis=0, tiled=True)
        width = x.shape[1] // pieces
        return [
            lax.all_gather(x[:, k * width : (k + 1) * width], names[-1], axis=0, tiled=True)
            for k in range(pieces)
        ]

    def scatter_sites(x):
        for stage in scatter_stages:
            x = lax.psum_scatter(x, stage, scatter_dimension=0, tiled=True)
        return x

    def gather_sites(x):
        for stage in reversed(scatter_stages):
            x = lax.all_gather(x, stage, axis=0, tiled=True)
        return x

    def on_device(activations, out_grads, theta, token_ids, assignment):
        head_cols = HEADS * HEAD_DIM
        site_ids = lax.all_gather(token_ids, shard_names, axis=0, tiled=True)
        acts_pieces = gather_events(to_position_order(activations, 1), FEATURE_PIECES)
        grad_cols = lax.all_to_all(out_grads, shard_names, split_axis=1, concat_axis=0, tiled=True)
        theta_rows = to_position_order(theta[0], 0)
        site_events = acts_pieces[0].shape[0]
        micro_rows = site_events // MICRO
        ordering = assignment[0]
        counts = count_same(site_ids)
        weights = 1.0 / counts.astype(jnp.float32)
        scaled = (grad_cols.astype(jnp.float32) * weights[:, None]).astype(jnp.bfloat16)
        position_batch = (jnp.arange(site_events, dtype=jnp.int32) // micro_rows)[None, :]
        hit = ordering[None, :] == jnp.arange(site_events, dtype=jnp.int32)[:, None]
        batch_of = jnp.sum(jnp.where(hit, position_batch, 0), axis=1)
        masked = jnp.concatenate(
            [jnp.where((batch_of == m)[:, None], scaled, jnp.zeros_like(scaled)) for m in range(MICRO)],
            axis=1,
        )
        cols = scaled.shape[1]
        blocks = []
        row_start = 0
        for piece in acts_pieces:
            gradients = lax.dot_general(
                piece, masked, (((0,), (0,)), ((), ())), preferred_element_type=jnp.float32
            )
            fisher = gradients[:, :cols] * gradients[:, :cols]
            for micro in range(1, MICRO):
                g = gradients[:, micro * cols : (micro + 1) * cols]
                fisher = fisher + g * g
            fisher = fisher / MICRO
            rows = piece.shape[1]
            product = fisher * theta_rows[row_start : row_start + rows].astype(jnp.float32)
            row_start += rows
            blocks.append(
                jnp.concatenate([product.astype(jnp.bfloat16), fisher.astype(jnp.bfloat16)], axis=1)
            )
        both = jnp.concatenate(blocks, axis=0)
        summed = scatter_sites(both).astype(jnp.float32)
        numerator, denominator = summed[:, :cols], summed[:, cols:]
        owned = (numerator / (denominator + epsilon)).astype(jnp.bfloat16)
        whole_merged = gather_sites(owned)
        scaling = float(head_cols) ** (-0.5)
        probe = jnp.concatenate(
            [jnp.take(piece, ordering[:micro_rows], axis=0) for piece in acts_pieces], axis=1
        )
        response = (
            jnp.dot(probe, whole_merged, preferred_element_type=jnp.float32) * scaling
        ).astype(jnp.bfloat16)
        return (owned, response)

    return on_device


def solution(mesh):
    sizes = dict(mesh.shape)
    site_ok = math.prod(s for _, s in SITE_SUB) == sizes["site"]
    shard_ok = math.prod(s for _, s in SHARD_SUB) == sizes["shard"]
    if site_ok and shard_ok:
        site_axes, shard_axes = SITE_SUB, SHARD_SUB
        scatter_stages = SCATTER_STAGES
        shape = tuple(s for _, s in SITE_SUB + SHARD_SUB)
        names = tuple(n for n, _ in SITE_SUB + SHARD_SUB)
        use_mesh = Mesh(np.asarray(mesh.devices).reshape(shape), names)
    else:
        site_axes, shard_axes = (("site", sizes["site"]),), (("shard", sizes["shard"]),)
        scatter_stages = (("site",),)
        use_mesh = mesh
    site = tuple(n for n, _ in site_axes)
    shard = tuple(n for n, _ in shard_axes)
    placed = (
        P(site + shard, None),
        P(site + shard, None),
        P(site, None, shard),
        P(site + shard),
        P(site, None),
    )
    return jax.shard_map(
        make_body(site_axes, shard_axes, scatter_stages),
        mesh=use_mesh,
        in_specs=placed,
        out_specs=(P(site, shard), P(site, shard)),
        check_vma=False,
    )
```

```python
import math

import jax
import jax.numpy as jnp
import numpy as np
from jax import lax
from jax.sharding import Mesh
from jax.sharding import PartitionSpec as P

HEADS = 20
HEAD_DIM = 128
MICRO = 4


epsilon = 1e-06

SITE_SUB = (("zh", 4), ("y", 4), ("c", 2))
SHARD_SUB = (("x", 4), ("zl", 4))
SCATTER_STAGES = (("y", "c"), ("zh",))


def count_same(site_ids):
    site_events = site_ids.shape[0]
    block_rows = math.gcd(site_events, 512)
    blocks = site_ids.reshape(site_events // block_rows, block_rows)

    def one_block(block_ids):
        return jnp.sum((block_ids[:, None] == site_ids[None, :]).astype(jnp.int32), axis=1)

    return lax.map(one_block, blocks).reshape(site_events)


def make_body(site_axes, shard_axes, scatter_stages):
    site_names = tuple(n for n, _ in site_axes)
    site_sizes = tuple(s for _, s in site_axes)
    shard_names = tuple(n for n, _ in shard_axes)
    position_names = tuple(n for stage in scatter_stages for n in stage)
    position_axes = tuple(site_names.index(n) for n in position_names)
    n_sub = len(site_sizes)

    def to_position_order(x, axis):
        shape = x.shape
        block = shape[axis] // math.prod(site_sizes)
        x = x.reshape(shape[:axis] + site_sizes + (block,) + shape[axis + 1 :])
        order = (
            tuple(range(axis))
            + tuple(axis + a for a in position_axes)
            + tuple(range(axis + n_sub, x.ndim))
        )
        return jnp.transpose(x, order).reshape(shape)

    def all_to_all_gather(x, names):
        group = math.prod(size for name, size in shard_axes if name in names)
        copies = jnp.broadcast_to(x[None], (group,) + x.shape)
        gathered = lax.all_to_all(copies, names, 0, 0, tiled=True)
        return gathered.reshape((group * x.shape[0],) + x.shape[1:])

    def gather_events(x):
        names = tuple(reversed(shard_names))
        x = all_to_all_gather(x, names[0])
        for name in names[1:]:
            x = lax.all_gather(x, name, axis=0, tiled=True)
        return x

    def scatter_sites(x):
        for stage in scatter_stages:
            x = lax.psum_scatter(x, stage, scatter_dimension=0, tiled=True)
        return x

    def gather_sites(x):
        for stage in reversed(scatter_stages):
            x = lax.all_gather(x, stage, axis=0, tiled=True)
        return x

    def on_device(activations, out_grads, theta, token_ids, assignment):
        head_cols = HEADS * HEAD_DIM
        site_ids = all_to_all_gather(token_ids, shard_names)
        site_acts = gather_events(to_position_order(activations, 1))
        grad_cols = lax.all_to_all(out_grads, shard_names, split_axis=1, concat_axis=0, tiled=True)
        theta_rows = to_position_order(theta[0], 0)
        site_events = site_acts.shape[0]
        micro_rows = site_events // MICRO
        ordering = assignment[0]
        counts = count_same(site_ids)
        weights = 1.0 / counts.astype(jnp.float32)
        scaled = (grad_cols.astype(jnp.float32) * weights[:, None]).astype(jnp.bfloat16)
        position_batch = (jnp.arange(site_events, dtype=jnp.int32) // micro_rows)[None, :]
        hit = ordering[None, :] == jnp.arange(site_events, dtype=jnp.int32)[:, None]
        batch_of = jnp.sum(jnp.where(hit, position_batch, 0), axis=1)
        masked = jnp.concatenate(
            [jnp.where((batch_of == m)[:, None], scaled, jnp.zeros_like(scaled)) for m in range(MICRO)],
            axis=1,
        )
        gradients = lax.dot_general(
            site_acts, masked, (((0,), (0,)), ((), ())), preferred_element_type=jnp.float32
        )
        cols = scaled.shape[1]
        fisher = gradients[:, :cols] * gradients[:, :cols]
        for micro in range(1, MICRO):
            g = gradients[:, micro * cols : (micro + 1) * cols]
            fisher = fisher + g * g
        fisher = fisher / MICRO
        product = fisher * theta_rows.astype(jnp.float32)
        both = jnp.concatenate([product.astype(jnp.bfloat16), fisher.astype(jnp.bfloat16)], axis=1)
        summed = scatter_sites(both).astype(jnp.float32)
        numerator, denominator = summed[:, :cols], summed[:, cols:]
        owned = (numerator / (denominator + epsilon)).astype(jnp.bfloat16)
        whole_merged = gather_sites(owned)
        scaling = float(head_cols) ** (-0.5)
        probe = jnp.take(site_acts, ordering[:micro_rows], axis=0)
        response = (
            jnp.dot(probe, whole_merged, preferred_element_type=jnp.float32) * scaling
        ).astype(jnp.bfloat16)
        return (owned, response)

    return on_device


def solution(mesh):
    sizes = dict(mesh.shape)
    site_ok = math.prod(s for _, s in SITE_SUB) == sizes["site"]
    shard_ok = math.prod(s for _, s in SHARD_SUB) == sizes["shard"]
    if site_ok and shard_ok:
        site_axes, shard_axes = SITE_SUB, SHARD_SUB
        scatter_stages = SCATTER_STAGES
        shape = tuple(s for _, s in SITE_SUB + SHARD_SUB)
        names = tuple(n for n, _ in SITE_SUB + SHARD_SUB)
        use_mesh = Mesh(np.asarray(mesh.devices).reshape(shape), names)
    else:
        site_axes, shard_axes = (("site", sizes["site"]),), (("shard", sizes["shard"]),)
        scatter_stages = (("site",),)
        use_mesh = mesh
    site = tuple(n for n, _ in site_axes)
    shard = tuple(n for n, _ in shard_axes)
    placed = (
        P(site + shard, None),
        P(site + shard, None),
        P(site, None, shard),
        P(site + shard),
        P(site, None),
    )
    return jax.shard_map(
        make_body(site_axes, shard_axes, scatter_stages),
        mesh=use_mesh,
        in_specs=placed,
        out_specs=(P(site, shard), P(site, shard)),
        check_vma=False,
    )
```

```python
import math

import jax
import jax.numpy as jnp
import numpy as np
from jax import lax
from jax.experimental.layout import Layout, with_layout_constraint
from jax.sharding import Mesh
from jax.sharding import PartitionSpec as P

HEADS = 20
HEAD_DIM = 128
MICRO = 4


epsilon = 1e-06

SITE_SUB = (("zh", 4), ("y", 4), ("c", 2))
SHARD_SUB = (("x", 4), ("zl", 4))
SCATTER_STAGES = (("y", "c"), ("zh",))


def count_same(site_ids):
    site_events = site_ids.shape[0]
    block_rows = math.gcd(site_events, 512)
    blocks = site_ids.reshape(site_events // block_rows, block_rows)

    def one_block(block_ids):
        return jnp.sum((block_ids[:, None] == site_ids[None, :]).astype(jnp.int32), axis=1)

    return lax.map(one_block, blocks).reshape(site_events)


def make_body(site_axes, shard_axes, scatter_stages):
    site_names = tuple(n for n, _ in site_axes)
    site_sizes = tuple(s for _, s in site_axes)
    shard_names = tuple(n for n, _ in shard_axes)
    position_names = tuple(n for stage in scatter_stages for n in stage)
    position_axes = tuple(site_names.index(n) for n in position_names)
    n_sub = len(site_sizes)

    def to_position_order(x, axis):
        shape = x.shape
        block = shape[axis] // math.prod(site_sizes)
        x = x.reshape(shape[:axis] + site_sizes + (block,) + shape[axis + 1 :])
        order = (
            tuple(range(axis))
            + tuple(axis + a for a in position_axes)
            + tuple(range(axis + n_sub, x.ndim))
        )
        return jnp.transpose(x, order).reshape(shape)

    def gather_events(x):
        for name in reversed(shard_names):
            x = lax.all_gather(x, name, axis=0, tiled=True)
        return x

    def scatter_sites(x):
        for stage in scatter_stages:
            x = lax.psum_scatter(x, stage, scatter_dimension=0, tiled=True)
        return x

    def gather_sites(x):
        for stage in reversed(scatter_stages):
            x = lax.all_gather(x, stage, axis=0, tiled=True)
        return x

    def on_device(activations, out_grads, theta, token_ids, assignment):
        head_cols = HEADS * HEAD_DIM
        site_ids = lax.all_gather(token_ids, shard_names, axis=0, tiled=True)
        site_acts = gather_events(to_position_order(activations, 1))
        grad_cols = lax.all_to_all(out_grads, shard_names, split_axis=1, concat_axis=0, tiled=True)
        theta_rows = to_position_order(theta[0], 0)
        site_events = site_acts.shape[0]
        micro_rows = site_events // MICRO
        ordering = assignment[0]
        counts = count_same(site_ids)
        weights = 1.0 / counts.astype(jnp.float32)
        scaled = (grad_cols.astype(jnp.float32) * weights[:, None]).astype(jnp.bfloat16)
        position_batch = (jnp.arange(site_events, dtype=jnp.int32) // micro_rows)[None, :]
        hit = ordering[None, :] == jnp.arange(site_events, dtype=jnp.int32)[:, None]
        batch_of = jnp.sum(jnp.where(hit, position_batch, 0), axis=1)
        masked = jnp.concatenate(
            [jnp.where((batch_of == m)[:, None], scaled, jnp.zeros_like(scaled)) for m in range(MICRO)],
            axis=1,
        )
        gradients = lax.dot_general(
            site_acts, masked, (((0,), (0,)), ((), ())), preferred_element_type=jnp.float32
        )
        cols = scaled.shape[1]
        fisher = gradients[:, :cols] * gradients[:, :cols]
        for micro in range(1, MICRO):
            g = gradients[:, micro * cols : (micro + 1) * cols]
            fisher = fisher + g * g
        fisher = fisher / MICRO
        product = fisher * theta_rows.astype(jnp.float32)
        both = jnp.concatenate([product.astype(jnp.bfloat16), fisher.astype(jnp.bfloat16)], axis=1)
        both = with_layout_constraint(both, Layout(major_to_minor=(0, 1)))
        summed = scatter_sites(both).astype(jnp.float32)
        numerator, denominator = summed[:, :cols], summed[:, cols:]
        owned = (numerator / (denominator + epsilon)).astype(jnp.bfloat16)
        whole_merged = gather_sites(owned)
        scaling = float(head_cols) ** (-0.5)
        probe = jnp.take(site_acts, ordering[:micro_rows], axis=0)
        response = (
            jnp.dot(probe, whole_merged, preferred_element_type=jnp.float32) * scaling
        ).astype(jnp.bfloat16)
        return (owned, response)

    return on_device


def solution(mesh):
    sizes = dict(mesh.shape)
    site_ok = math.prod(s for _, s in SITE_SUB) == sizes["site"]
    shard_ok = math.prod(s for _, s in SHARD_SUB) == sizes["shard"]
    if site_ok and shard_ok:
        site_axes, shard_axes = SITE_SUB, SHARD_SUB
        scatter_stages = SCATTER_STAGES
        shape = tuple(s for _, s in SITE_SUB + SHARD_SUB)
        names = tuple(n for n, _ in SITE_SUB + SHARD_SUB)
        use_mesh = Mesh(np.asarray(mesh.devices).reshape(shape), names)
    else:
        site_axes, shard_axes = (("site", sizes["site"]),), (("shard", sizes["shard"]),)
        scatter_stages = (("site",),)
        use_mesh = mesh
    site = tuple(n for n, _ in site_axes)
    shard = tuple(n for n, _ in shard_axes)
    placed = (
        P(site + shard, None),
        P(site + shard, None),
        P(site, None, shard),
        P(site + shard),
        P(site, None),
    )
    return jax.shard_map(
        make_body(site_axes, shard_axes, scatter_stages),
        mesh=use_mesh,
        in_specs=placed,
        out_specs=(P(site, shard), P(site, shard)),
        check_vma=False,
    )
```

```python
import math

import jax
import jax.numpy as jnp
import numpy as np
from jax import lax
from jax.sharding import Mesh
from jax.sharding import PartitionSpec as P

HEADS = 20
HEAD_DIM = 128
MICRO = 4


epsilon = 1e-06

SITE_SUB = (("zh", 4), ("y", 4), ("c", 2))
SHARD_SUB = (("x", 4), ("zl", 4))
SCATTER_STAGES = (("y", "c"), ("zh",))


def count_same(site_ids):
    site_events = site_ids.shape[0]
    block_rows = math.gcd(site_events, 512)
    blocks = site_ids.reshape(site_events // block_rows, block_rows)

    def one_block(block_ids):
        return jnp.sum((block_ids[:, None] == site_ids[None, :]).astype(jnp.int32), axis=1)

    return lax.map(one_block, blocks).reshape(site_events)


def make_body(site_axes, shard_axes, scatter_stages):
    site_names = tuple(n for n, _ in site_axes)
    site_sizes = tuple(s for _, s in site_axes)
    shard_names = tuple(n for n, _ in shard_axes)
    position_names = tuple(n for stage in scatter_stages for n in stage)
    position_axes = tuple(site_names.index(n) for n in position_names)
    n_sub = len(site_sizes)

    def to_position_order(x, axis):
        shape = x.shape
        block = shape[axis] // math.prod(site_sizes)
        x = x.reshape(shape[:axis] + site_sizes + (block,) + shape[axis + 1 :])
        order = (
            tuple(range(axis))
            + tuple(axis + a for a in position_axes)
            + tuple(range(axis + n_sub, x.ndim))
        )
        return jnp.transpose(x, order).reshape(shape)

    def gather_events(x):
        for name in reversed(shard_names):
            x = lax.all_gather(x, name, axis=0, tiled=True)
        return x

    def scatter_sites(x):
        for stage in scatter_stages:
            x = lax.psum_scatter(x, stage, scatter_dimension=0, tiled=True)
        return x

    def gather_sites(x):
        stages = tuple(reversed(scatter_stages))
        group = math.prod(size for name, size in site_axes if name in stages[0])
        copies = jnp.broadcast_to(x[None], (group,) + x.shape)
        x = lax.all_to_all(copies, stages[0], 0, 0, tiled=True).reshape((group * x.shape[0],) + x.shape[1:])
        for stage in stages[1:]:
            x = lax.all_gather(x, stage, axis=0, tiled=True)
        return x

    def on_device(activations, out_grads, theta, token_ids, assignment):
        head_cols = HEADS * HEAD_DIM
        site_ids = lax.all_gather(token_ids, shard_names, axis=0, tiled=True)
        site_acts = gather_events(to_position_order(activations, 1))
        grad_cols = lax.all_to_all(out_grads, shard_names, split_axis=1, concat_axis=0, tiled=True)
        theta_rows = to_position_order(theta[0], 0)
        site_events = site_acts.shape[0]
        micro_rows = site_events // MICRO
        ordering = assignment[0]
        counts = count_same(site_ids)
        weights = 1.0 / counts.astype(jnp.float32)
        scaled = (grad_cols.astype(jnp.float32) * weights[:, None]).astype(jnp.bfloat16)
        position_batch = (jnp.arange(site_events, dtype=jnp.int32) // micro_rows)[None, :]
        hit = ordering[None, :] == jnp.arange(site_events, dtype=jnp.int32)[:, None]
        batch_of = jnp.sum(jnp.where(hit, position_batch, 0), axis=1)
        masked = jnp.concatenate(
            [jnp.where((batch_of == m)[:, None], scaled, jnp.zeros_like(scaled)) for m in range(MICRO)],
            axis=1,
        )
        gradients = lax.dot_general(
            site_acts, masked, (((0,), (0,)), ((), ())), preferred_element_type=jnp.float32
        )
        cols = scaled.shape[1]
        fisher = gradients[:, :cols] * gradients[:, :cols]
        for micro in range(1, MICRO):
            g = gradients[:, micro * cols : (micro + 1) * cols]
            fisher = fisher + g * g
        fisher = fisher / MICRO
        product = fisher * theta_rows.astype(jnp.float32)
        both = jnp.concatenate([product.astype(jnp.bfloat16), fisher.astype(jnp.bfloat16)], axis=1)
        summed = scatter_sites(both).astype(jnp.float32)
        numerator, denominator = summed[:, :cols], summed[:, cols:]
        owned = (numerator / (denominator + epsilon)).astype(jnp.bfloat16)
        whole_merged = gather_sites(owned)
        scaling = float(head_cols) ** (-0.5)
        probe = jnp.take(site_acts, ordering[:micro_rows], axis=0)
        response = (
            jnp.dot(probe, whole_merged, preferred_element_type=jnp.float32) * scaling
        ).astype(jnp.bfloat16)
        return (owned, response)

    return on_device


def solution(mesh):
    sizes = dict(mesh.shape)
    site_ok = math.prod(s for _, s in SITE_SUB) == sizes["site"]
    shard_ok = math.prod(s for _, s in SHARD_SUB) == sizes["shard"]
    if site_ok and shard_ok:
        site_axes, shard_axes = SITE_SUB, SHARD_SUB
        scatter_stages = SCATTER_STAGES
        shape = tuple(s for _, s in SITE_SUB + SHARD_SUB)
        names = tuple(n for n, _ in SITE_SUB + SHARD_SUB)
        use_mesh = Mesh(np.asarray(mesh.devices).reshape(shape), names)
    else:
        site_axes, shard_axes = (("site", sizes["site"]),), (("shard", sizes["shard"]),)
        scatter_stages = (("site",),)
        use_mesh = mesh
    site = tuple(n for n, _ in site_axes)
    shard = tuple(n for n, _ in shard_axes)
    placed = (
        P(site + shard, None),
        P(site + shard, None),
        P(site, None, shard),
        P(site + shard),
        P(site, None),
    )
    return jax.shard_map(
        make_body(site_axes, shard_axes, scatter_stages),
        mesh=use_mesh,
        in_specs=placed,
        out_specs=(P(site, shard), P(site, shard)),
        check_vma=False,
    )
```

```python
import math

import jax
import jax.numpy as jnp
import numpy as np
from jax import lax
from jax.sharding import Mesh
from jax.sharding import PartitionSpec as P

HEADS = 20
HEAD_DIM = 128
MICRO = 4


epsilon = 1e-06

SITE_SUB = (("zh", 4), ("y", 4), ("c", 2))
SHARD_SUB = (("x", 4), ("zl", 4))
SCATTER_STAGES = (("y", "c"), ("zh",))


def count_same(site_ids):
    site_events = site_ids.shape[0]
    block_rows = math.gcd(site_events, 512)
    blocks = site_ids.reshape(site_events // block_rows, block_rows)

    def one_block(block_ids):
        return jnp.sum((block_ids[:, None] == site_ids[None, :]).astype(jnp.int32), axis=1)

    return lax.map(one_block, blocks).reshape(site_events)


def make_body(site_axes, shard_axes, scatter_stages):
    site_names = tuple(n for n, _ in site_axes)
    site_sizes = tuple(s for _, s in site_axes)
    shard_names = tuple(n for n, _ in shard_axes)
    position_names = tuple(n for stage in scatter_stages for n in stage)
    position_axes = tuple(site_names.index(n) for n in position_names)
    n_sub = len(site_sizes)

    def to_position_order(x, axis):
        shape = x.shape
        block = shape[axis] // math.prod(site_sizes)
        x = x.reshape(shape[:axis] + site_sizes + (block,) + shape[axis + 1 :])
        order = (
            tuple(range(axis))
            + tuple(axis + a for a in position_axes)
            + tuple(range(axis + n_sub, x.ndim))
        )
        return jnp.transpose(x, order).reshape(shape)

    def gather_events(x):
        for name in reversed(shard_names):
            x = lax.all_gather(x, name, axis=0, tiled=True)
        return x

    def scatter_sites(x):
        for stage in scatter_stages:
            x = lax.psum_scatter(x, stage, scatter_dimension=0, tiled=True)
        return x

    def gather_sites(x):
        for stage in reversed(scatter_stages):
            x = lax.all_gather(x, stage, axis=0, tiled=True)
        return x

    def on_device(activations, out_grads, theta, token_ids, assignment):
        head_cols = HEADS * HEAD_DIM
        group = math.prod(size for _, size in shard_axes)
        id_copies = jnp.broadcast_to(token_ids[None], (group,) + token_ids.shape)
        site_ids = lax.all_to_all(id_copies, shard_names, 0, 0, tiled=True).reshape(-1)
        site_acts = gather_events(to_position_order(activations, 1))
        grad_cols = lax.all_to_all(out_grads, shard_names, split_axis=1, concat_axis=0, tiled=True)
        theta_rows = to_position_order(theta[0], 0)
        site_events = site_acts.shape[0]
        micro_rows = site_events // MICRO
        ordering = assignment[0]
        counts = count_same(site_ids)
        weights = 1.0 / counts.astype(jnp.float32)
        scaled = (grad_cols.astype(jnp.float32) * weights[:, None]).astype(jnp.bfloat16)
        position_batch = (jnp.arange(site_events, dtype=jnp.int32) // micro_rows)[None, :]
        hit = ordering[None, :] == jnp.arange(site_events, dtype=jnp.int32)[:, None]
        batch_of = jnp.sum(jnp.where(hit, position_batch, 0), axis=1)
        masked = jnp.concatenate(
            [jnp.where((batch_of == m)[:, None], scaled, jnp.zeros_like(scaled)) for m in range(MICRO)],
            axis=1,
        )
        gradients = lax.dot_general(
            site_acts, masked, (((0,), (0,)), ((), ())), preferred_element_type=jnp.float32
        )
        cols = scaled.shape[1]
        fisher = gradients[:, :cols] * gradients[:, :cols]
        for micro in range(1, MICRO):
            g = gradients[:, micro * cols : (micro + 1) * cols]
            fisher = fisher + g * g
        fisher = fisher / MICRO
        product = fisher * theta_rows.astype(jnp.float32)
        both = jnp.concatenate([product.astype(jnp.bfloat16), fisher.astype(jnp.bfloat16)], axis=1)
        summed = scatter_sites(both).astype(jnp.float32)
        numerator, denominator = summed[:, :cols], summed[:, cols:]
        owned = (numerator / (denominator + epsilon)).astype(jnp.bfloat16)
        whole_merged = gather_sites(owned)
        scaling = float(head_cols) ** (-0.5)
        probe = jnp.take(site_acts, ordering[:micro_rows], axis=0)
        response = (
            jnp.dot(probe, whole_merged, preferred_element_type=jnp.float32) * scaling
        ).astype(jnp.bfloat16)
        return (owned, response)

    return on_device


def solution(mesh):
    sizes = dict(mesh.shape)
    site_ok = math.prod(s for _, s in SITE_SUB) == sizes["site"]
    shard_ok = math.prod(s for _, s in SHARD_SUB) == sizes["shard"]
    if site_ok and shard_ok:
        site_axes, shard_axes = SITE_SUB, SHARD_SUB
        scatter_stages = SCATTER_STAGES
        shape = tuple(s for _, s in SITE_SUB + SHARD_SUB)
        names = tuple(n for n, _ in SITE_SUB + SHARD_SUB)
        use_mesh = Mesh(np.asarray(mesh.devices).reshape(shape), names)
    else:
        site_axes, shard_axes = (("site", sizes["site"]),), (("shard", sizes["shard"]),)
        scatter_stages = (("site",),)
        use_mesh = mesh
    site = tuple(n for n, _ in site_axes)
    shard = tuple(n for n, _ in shard_axes)
    placed = (
        P(site + shard, None),
        P(site + shard, None),
        P(site, None, shard),
        P(site + shard),
        P(site, None),
    )
    return jax.shard_map(
        make_body(site_axes, shard_axes, scatter_stages),
        mesh=use_mesh,
        in_specs=placed,
        out_specs=(P(site, shard), P(site, shard)),
        check_vma=False,
    )
```
